1024 devices in a mesh: ctx: 16 (over z_hi, y), seq: 32 (over x, z_lo), head: 2 (over core).
Axes of the slice: x: 4, y: 4, z: 32 (z_hi: 4, z_lo: 8; z = z_hi * 8 + z_lo), core: 2. Of those that a mesh axis runs over, the one named last changes fastest.
Arguments:
- queries: bfloat16 [32, 2048, 4096], P('seq', 'ctx', 'head'), may hold values from -6 to 6
- keys_values: bfloat16 [32, 2048, 4, 256], P('seq', 'ctx', 'head'), may hold values from -6 to 6
- out_grad: bfloat16 [32, 2048, 4096], P('seq', 'ctx', 'head'), may hold values from -24 to 24
- doc_ids: int32 [32, 2048], P('seq'), may hold values from 0 to 15, never falling along the last dimension, each value on 1 to 256 neighbouring positions
- route: int32 [16, 32, 2], P('ctx'), may hold values from 0 to 31, as said below
Outputs:
- query_grad: bfloat16 [32, 2048, 4096], P('seq', 'ctx', 'head')
- kv_grad_owned: bfloat16 [32, 4096, 4, 256], P('seq', 'ctx', 'head')
The draws below stay inside these ranges and needn't reach their ends.
Inputs may be any that keep to these rules, and one draw needn't show every extreme that they name: `doc_ids`: each document covers at most 256 consecutive positions, and one covers exactly that many. `route`: for each block index, the 2 pieces of one stretch go to distinct owners; an owner receives at most 4 pieces of one block index, and in every block index some owner receives exactly that many.
All inputs are finite; a program needn't handle non-finite values.
Results may differ from the reference program's by a relative error of at most 0.0057.
Values may be sent and summed in bfloat16 or wider, within the bound.
No kernel may reach another device: no remote copies, remote signals or barrier semaphores. Data moves between devices by JAX's collectives and lax.ppermute only.
A program may use at most 32 MiB of HBM per device.

```python
import math
import jax
import jax.numpy as jnp
import numpy as np
from jax import lax

HD = 128
HEADS = 32
KV = 4
TOK_DEV = 128
PIECE = 64
REACH = 3
PIECES = 2
SEQS = 32
CTXS = 16
LENGTH = 2048
OWN_ROWS = 256
DOCS = 16
DOC_MOST = 256


def draw_route(key, part):

    def one_row(row_key):
        parts_keys = jax.random.split(row_key, 4)
        source_perm = jax.random.permutation(parts_keys[0], SEQS).astype(jnp.int32)
        owner_perm = jax.random.permutation(parts_keys[1], SEQS).astype(jnp.int32)
        merged = jax.random.randint(parts_keys[2], (PIECES, SEQS // 2), 0, 2).astype(jnp.int32)
        toward = jax.random.randint(parts_keys[3], (PIECES, SEQS // 2), 0, 2).astype(jnp.int32)
        merged = merged.at[:, 0].set(1)
        toward = toward.at[:, 0].set(0)
        piece_index = jnp.arange(PIECES, dtype=jnp.int32)
        target = (source_perm[:, None] + piece_index[None, :] * (SEQS // PIECES)) % SEQS
        pair_ids = target // 2
        merged_at = merged[piece_index[None, :], pair_ids]
        toward_at = toward[piece_index[None, :], pair_ids]
        final = jnp.where(merged_at == 1, 2 * pair_ids + toward_at, target)
        return owner_perm[final]
    return jax.vmap(one_row)(jax.random.split(key, CTXS)).astype(jnp.int32)


def shard_levels(own_key, extent, shards, smallest, high):
    gain, own = 1.0, jax.random.fold_in(own_key, 6)
    for position, parts in shards:
        steps = jnp.exp(jax.random.uniform(jax.random.fold_in(own, position), (parts,), jnp.float32, smallest / len(shards), high / len(shards)))
        gain = gain * jnp.repeat(steps, extent[position] // parts).reshape([-1 if axis == position else 1 for axis in range(len(extent))])
    return gain


def split_up(amount, total, reach, skew):
    loads = [(1 << 20) // math.isqrt(standing ** skew) + 1 for standing in range(2, amount + 1)]
    surplus, counts = total - reach - (amount - 1), [1] * (amount - 1)
    while surplus > 0:
        free = [i for i in range(amount - 1) if counts[i] < reach]
        whole, left = sum([loads[i] for i in free]), surplus
        for i in free:
            more = min(reach - counts[i], max(1, left * loads[i] // whole), surplus)
            counts[i] = counts[i] + more
            surplus = surplus - more
    return np.array([reach] + counts)


def uneven(rng, count, total, limit, lean):
    if count == 2:
        one = jax.random.randint(rng, (), max(1, total - limit), min(limit, total - 1) + 1)
        return jnp.stack([one, total - one])
    tallies = jnp.asarray(split_up(count, total, limit, lean), jnp.int32)
    pairs = (count - 1) // 2
    giver, taker = tallies[1:1 + 2 * pairs:2], tallies[2:2 + 2 * pairs:2]
    margin = jnp.minimum(giver - 1, limit - taker)
    shifted = jax.random.randint(jax.random.fold_in(rng, 1), (pairs,), 0, 1 << 20) % (margin + 1)
    tallies = tallies.at[1:1 + 2 * pairs:2].set(giver - shifted).at[2:2 + 2 * pairs:2].set(taker + shifted)
    return tallies[jax.random.permutation(jax.random.fold_in(rng, 2), count)]


def gaussian(own_key, extent, scale, bound, cuts=(), held_as=jnp.bfloat16):
    drawn = scale * jax.random.normal(own_key, extent, jnp.float32)
    if cuts:
        drawn = drawn * shard_levels(own_key, extent, cuts, -0.22, 0.18)
    return jnp.clip(drawn, -bound, bound).astype(held_as)


def setup_inputs(seed: int = 0) -> dict:
    streams_of = jax.random.split(jax.random.key(seed), 6)
    queries = gaussian(streams_of[0], (SEQS, LENGTH, HEADS * HD), 1.0, 6.0, ((0, 32), (1, 16), (2, 2)))
    keys_values = gaussian(streams_of[1], (SEQS, LENGTH, KV, 2 * HD), 1.0, 6.0, ((0, 32), (1, 16), (2, 2)))
    out_grad = gaussian(streams_of[2], (SEQS, LENGTH, HEADS * HD), 4.0, 24.0, ((0, 32), (1, 16), (2, 2)))
    doc_ids = jax.vmap(lambda own: jnp.searchsorted(jnp.cumsum(uneven(own, DOCS, LENGTH, DOC_MOST, 1)), jnp.arange(LENGTH), side="right"))(jax.random.split(streams_of[3], SEQS)).reshape((SEQS, LENGTH)).astype(jnp.int32)
    route = draw_route(jax.random.fold_in(streams_of[5], 71), 0)
    return {"queries": queries, "keys_values": keys_values, "out_grad": out_grad, "doc_ids": doc_ids, "route": route}


def round_low(values):
    return lax.optimization_barrier(values.astype(jnp.bfloat16)).astype(jnp.float32)


def reference(queries, keys_values, out_grad, doc_ids, route):
    group_size = HEADS // KV
    scale_factor = HD ** -0.5
    reach_rows = REACH * TOK_DEV
    front_rows = (REACH - 1) * TOK_DEV
    offsets = jnp.arange(TOK_DEV, dtype=jnp.int32)
    window_offsets = jnp.arange(reach_rows, dtype=jnp.int32)

    def one_sequence(operands):
        seq_queries, seq_kv, seq_grad, seq_docs = operands
        padded_kv = jnp.concatenate([jnp.zeros((front_rows, KV, 2 * HD), jnp.bfloat16), seq_kv], 0)
        padded_docs = jnp.concatenate([jnp.full((front_rows,), -1, jnp.int32), seq_docs.astype(jnp.int32)], 0)

        def one_block(grad_kv, block):
            start = (block * TOK_DEV).astype(jnp.int32)
            query_rows = lax.dynamic_slice_in_dim(seq_queries, start, TOK_DEV, 0).astype(jnp.float32).reshape(TOK_DEV, KV, group_size, HD)
            grad_rows = lax.dynamic_slice_in_dim(seq_grad, start, TOK_DEV, 0).astype(jnp.float32).reshape(TOK_DEV, KV, group_size, HD)
            window = lax.dynamic_slice_in_dim(padded_kv, start, reach_rows, 0).astype(jnp.float32)
            key_rows = window[..., :HD]
            value_rows = window[..., HD:]
            query_doc = lax.dynamic_slice_in_dim(seq_docs.astype(jnp.int32), start, TOK_DEV, 0)
            key_doc = lax.dynamic_slice_in_dim(padded_docs, start, reach_rows, 0)
            query_pos = start + offsets
            key_pos = start - front_rows + window_offsets
            seen = (query_doc[:, None] == key_doc[None, :]) & (key_pos[None, :] <= query_pos[:, None]) & (key_pos[None, :] >= 0)
            scores = jnp.einsum('igad,jgd->gaij', query_rows, key_rows) * scale_factor
            exp_scores = jnp.where(seen[None, None], jnp.exp(scores), 0.0)
            totals = jnp.sum(exp_scores, -1)
            weights_low = round_low(exp_scores)
            attended = jnp.einsum('gaij,jgd->igad', weights_low, value_rows) / jnp.transpose(totals, (2, 0, 1))[..., None]
            delta = jnp.transpose(jnp.sum(grad_rows * attended, -1), (1, 2, 0))
            probs = exp_scores / totals[..., None]
            probs_low = round_low(probs)
            grad_probs = jnp.einsum('igad,jgd->gaij', grad_rows, value_rows)
            grad_scores = round_low(probs * (grad_probs - delta[..., None]))
            query_grad = jnp.einsum('gaij,jgd->igad', grad_scores, key_rows) * scale_factor
            key_grad = jnp.einsum('gaij,igad->jgd', grad_scores, query_rows) * scale_factor
            value_grad = jnp.einsum('gaij,igad->jgd', probs_low, grad_rows)
            both_grads = jnp.concatenate([key_grad, value_grad], -1)
            current = lax.dynamic_slice_in_dim(grad_kv, start, reach_rows, 0)
            grad_kv = lax.dynamic_update_slice_in_dim(grad_kv, current + both_grads, start, 0)
            return grad_kv, query_grad.reshape(TOK_DEV, HEADS * HD).astype(jnp.bfloat16)

        initial = jnp.zeros((front_rows + LENGTH, KV, 2 * HD), jnp.float32)
        grad_kv, query_blocks = lax.scan(one_block, initial, jnp.arange(CTXS, dtype=jnp.int32))
        return query_blocks.reshape(LENGTH, HEADS * HD), grad_kv[front_rows:].astype(jnp.bfloat16)

    query_grad, kv_grad = lax.map(one_sequence, (queries, keys_values, out_grad, doc_ids))
    pieces = kv_grad.reshape(SEQS, CTXS, PIECES, PIECE, KV, 2 * HD).astype(jnp.float32)
    owners = jnp.arange(SEQS, dtype=jnp.int32)
    chosen = (route.astype(jnp.int32)[:, :, :, None] == owners).astype(jnp.int32)
    sends = jnp.sum(chosen, 2)
    ranks = jnp.cumsum(sends, 1) - sends
    slots = jnp.arange(2 * PIECES, dtype=jnp.int32)
    assign = (chosen[..., None] * (ranks[:, :, None, :, None] == slots).astype(jnp.int32)).astype(jnp.float32)
    owned = jnp.einsum('cspok,scpxhw->ockxhw', assign, pieces)
    return query_grad, owned.reshape(SEQS, CTXS * OWN_ROWS, KV, 2 * HD).astype(jnp.bfloat16)
```

```python
import jax
import jax.numpy as jnp
from jax import lax
from jax.sharding import Mesh, PartitionSpec as P

HD = 128
PIECE = 64


def shifted(shard, axis, by):
    peers = lax.axis_size(axis)
    pairs = [(i, i + by) for i in range(peers) if 0 <= i + by < peers]
    return lax.ppermute(shard, axis, pairs)


def shards(queries, keys_values, out_grad, doc_ids, route):
    tok_rows = queries.shape[1]
    kv_heads = keys_values.shape[2]
    group_size = queries.shape[2] // HD // kv_heads
    ctx_index = lax.axis_index("ctx")
    reach_steps = min(3, lax.axis_size("ctx"))
    scale_factor = HD ** (-0.5)
    query_four = queries[0].reshape(tok_rows, kv_heads, group_size, HD)
    grad_four = out_grad[0].reshape(tok_rows, kv_heads, group_size, HD)
    kv_local = keys_values[0]
    doc_row = doc_ids[0]
    offsets = jnp.arange(tok_rows, dtype=jnp.int32)
    query_pos = ctx_index * tok_rows + offsets
    query_doc = lax.dynamic_slice_in_dim(doc_row, ctx_index * tok_rows, tok_rows, 0)
    kv_blocks = [kv_local] + [shifted(kv_local, "ctx", d) for d in range(1, reach_steps)]
    totals = jnp.zeros((kv_heads, group_size, tok_rows), jnp.float32)
    out_acc = jnp.zeros((tok_rows, kv_heads, group_size, HD), jnp.float32)
    saved_exp = []
    for distance in range(reach_steps):
        scores = (
            jnp.einsum(
                "igad,jgd->gaij",
                query_four,
                kv_blocks[distance][..., :HD],
                preferred_element_type=jnp.float32,
            )
            * scale_factor
        )
        source = ctx_index - distance
        key_pos = source * tok_rows + offsets
        key_doc = lax.dynamic_slice_in_dim(doc_row, jnp.maximum(source, 0) * tok_rows, tok_rows, 0)
        exp_scores = jnp.where(
            (
                (query_doc[:, None] == key_doc[None, :])
                & (key_pos[None, :] <= query_pos[:, None])
                & (key_pos[None, :] >= 0)
            )[None, None],
            jnp.exp(scores),
            0.0,
        )
        saved_exp.append(exp_scores)
        totals = totals + jnp.sum(exp_scores, -1)
        out_acc = out_acc + jnp.einsum(
            "gaij,jgd->igad",
            exp_scores.astype(jnp.bfloat16),
            kv_blocks[distance][..., HD:],
            preferred_element_type=jnp.float32,
        )
    attended = out_acc / jnp.transpose(totals, (2, 0, 1))[..., None]
    delta = jnp.transpose(jnp.sum(grad_four.astype(jnp.float32) * attended, -1), (1, 2, 0))
    dq_acc = jnp.zeros((tok_rows, kv_heads, group_size, HD), jnp.float32)
    kv_sum = None
    for distance in range(reach_steps):
        key_block = kv_blocks[distance][..., :HD]
        value_block = kv_blocks[distance][..., HD:]
        probs = saved_exp[distance] / totals[..., None]
        probs_low = probs.astype(jnp.bfloat16)
        grad_probs = jnp.einsum(
            "igad,jgd->gaij", grad_four, value_block, preferred_element_type=jnp.float32
        )
        score_low = (probs * (grad_probs - delta[..., None])).astype(jnp.bfloat16)
        dq_acc = dq_acc + jnp.einsum(
            "gaij,jgd->igad", score_low, key_block, preferred_element_type=jnp.float32
        )
        key_grad = (
            jnp.einsum("gaij,igad->jgd", score_low, query_four, preferred_element_type=jnp.float32)
            * scale_factor
        )
        value_grad = jnp.einsum(
            "gaij,igad->jgd", probs_low, grad_four, preferred_element_type=jnp.float32
        )
        term_kv = jnp.concatenate([key_grad, value_grad], -1)
        if distance > 0:
            term_kv = shifted(term_kv, "ctx", -distance)
        kv_sum = term_kv if kv_sum is None else kv_sum + term_kv
    query_grad = (
        (dq_acc * scale_factor)
        .astype(jnp.bfloat16)
        .reshape(1, tok_rows, kv_heads * group_size * HD)
    )
    kv_grad = kv_sum.astype(jnp.bfloat16)
    inner = lax.axis_size("sz")
    outer = lax.axis_size("sx")
    row_index = lax.axis_index("sx")
    col_index = lax.axis_index("sz")
    piece_count = tok_rows // PIECE
    route_table = route[0]
    seq_count = route_table.shape[0]
    piece_rows = kv_grad.reshape(piece_count, PIECE, kv_heads, 2 * HD)
    my_route = lax.dynamic_index_in_dim(route_table, row_index * inner + col_index, 0, keepdims=False)
    col_ids = jnp.arange(inner, dtype=jnp.int32)
    to_col = (my_route[None, :] % inner == col_ids[:, None]).astype(jnp.bfloat16)
    first_out = jnp.einsum(
        "cp,pxhw->cpxhw", to_col, piece_rows, preferred_element_type=jnp.bfloat16
    )
    first_in = lax.all_to_all(first_out, "sz", split_axis=0, concat_axis=0, tiled=True)
    row_routes = lax.dynamic_slice_in_dim(route_table, row_index * inner, inner, 0)
    owners = jnp.arange(seq_count, dtype=jnp.int32)
    hits = (route_table[:, :, None] == owners[None, None, :]).astype(jnp.int32)
    sends = jnp.sum(hits, 1)
    ranks = jnp.cumsum(sends, 0) - sends
    row_ranks = lax.dynamic_slice_in_dim(ranks, row_index * inner, inner, 0)
    slot_ids = jnp.arange(2 * piece_count, dtype=jnp.int32)
    target_rows = jnp.arange(outer, dtype=jnp.int32)
    target_owner = target_rows * inner + col_index
    piece_owner = row_routes
    piece_rank = jnp.take_along_axis(row_ranks, piece_owner, axis=1)
    second_map = (
        (piece_owner[None, None, :, :] == target_owner[:, None, None, None])
        & (piece_rank[None, None, :, :] == slot_ids[None, :, None, None])
    ).astype(jnp.bfloat16)
    second_out = jnp.einsum(
        "tkzp,zpxhw->tkxhw", second_map, first_in, preferred_element_type=jnp.float32
    ).astype(jnp.bfloat16)
    second_in = lax.all_to_all(second_out, "sx", split_axis=0, concat_axis=0, tiled=True)
    owned = jnp.sum(second_in.astype(jnp.float32), 0).astype(jnp.bfloat16)
    return (query_grad, owned.reshape(1, 2 * piece_count * PIECE, kv_heads, 2 * HD))


def solution(mesh):
    seq_count = mesh.shape["seq"]
    inner = 8 if seq_count % 8 == 0 else 1
    split_mesh = Mesh(
        mesh.devices.reshape(mesh.shape["ctx"], seq_count // inner, inner, mesh.shape["head"]),
        ("ctx", "sx", "sz", "head"),
    )
    seq = ("sx", "sz")
    placed = (
        P(seq, "ctx", "head"),
        P(seq, "ctx", "head", None),
        P(seq, "ctx", "head"),
        P(seq, None),
        P("ctx", None, None),
    )
    return jax.shard_map(
        shards,
        mesh=split_mesh,
        in_specs=placed,
        out_specs=(P(seq, "ctx", "head"), P(seq, "ctx", "head", None)),
        check_vma=False,
    )
```

```python
import jax
import jax.numpy as jnp
from jax import lax
from jax.sharding import Mesh, PartitionSpec as P

HD = 128
PIECE = 64


def shifted(shard, axis, by):
    peers = lax.axis_size(axis)
    pairs = [(i, i + by) for i in range(peers) if 0 <= i + by < peers]
    return lax.ppermute(shard, axis, pairs)


def shards(queries, keys_values, out_grad, doc_ids, route):
    tok_rows = queries.shape[1]
    kv_heads = keys_values.shape[2]
    group_size = queries.shape[2] // HD // kv_heads
    ctx_index = lax.axis_index("ctx")
    reach_steps = min(3, lax.axis_size("ctx"))
    scale_factor = HD ** (-0.5)
    query_four = queries[0].reshape(tok_rows, kv_heads, group_size, HD)
    grad_four = out_grad[0].reshape(tok_rows, kv_heads, group_size, HD)
    kv_local = keys_values[0]
    doc_row = doc_ids[0]
    offsets = jnp.arange(tok_rows, dtype=jnp.int32)
    query_pos = ctx_index * tok_rows + offsets
    query_doc = lax.dynamic_slice_in_dim(doc_row, ctx_index * tok_rows, tok_rows, 0)
    kv_blocks = [kv_local] + [shifted(kv_local, "ctx", d) for d in range(1, reach_steps)]
    totals = jnp.zeros((kv_heads, group_size, tok_rows), jnp.float32)
    out_acc = jnp.zeros((tok_rows, kv_heads, group_size, HD), jnp.float32)
    saved_exp = []
    for distance in range(reach_steps):
        scores = (
            jnp.einsum(
                "igad,jgd->gaij",
                query_four,
                kv_blocks[distance][..., :HD],
                preferred_element_type=jnp.float32,
            )
            * scale_factor
        )
        source = ctx_index - distance
        key_pos = source * tok_rows + offsets
        key_doc = lax.dynamic_slice_in_dim(doc_row, jnp.maximum(source, 0) * tok_rows, tok_rows, 0)
        exp_scores = jnp.where(
            (
                (query_doc[:, None] == key_doc[None, :])
                & (key_pos[None, :] <= query_pos[:, None])
                & (key_pos[None, :] >= 0)
            )[None, None],
            jnp.exp(scores),
            0.0,
        )
        saved_exp.append(exp_scores)
        totals = totals + jnp.sum(exp_scores, -1)
        out_acc = out_acc + jnp.einsum(
            "gaij,jgd->igad",
            exp_scores.astype(jnp.bfloat16),
            kv_blocks[distance][..., HD:],
            preferred_element_type=jnp.float32,
        )
    attended = out_acc / jnp.transpose(totals, (2, 0, 1))[..., None]
    delta = jnp.transpose(jnp.sum(grad_four.astype(jnp.float32) * attended, -1), (1, 2, 0))
    dq_acc = jnp.zeros((tok_rows, kv_heads, group_size, HD), jnp.float32)
    kv_sum = None
    for distance in range(reach_steps):
        key_block = kv_blocks[distance][..., :HD]
        value_block = kv_blocks[distance][..., HD:]
        probs = saved_exp[distance] / totals[..., None]
        probs_low = probs.astype(jnp.bfloat16)
        grad_probs = jnp.einsum(
            "igad,jgd->gaij", grad_four, value_block, preferred_element_type=jnp.float32
        )
        score_low = (probs * (grad_probs - delta[..., None])).astype(jnp.bfloat16)
        dq_acc = dq_acc + jnp.einsum(
            "gaij,jgd->igad", score_low, key_block, preferred_element_type=jnp.float32
        )
        key_grad = (
            jnp.einsum("gaij,igad->jgd", score_low, query_four, preferred_element_type=jnp.float32)
            * scale_factor
        )
        value_grad = jnp.einsum(
            "gaij,igad->jgd", probs_low, grad_four, preferred_element_type=jnp.float32
        )
        term_kv = jnp.concatenate([key_grad, value_grad], -1)
        if distance > 0:
            term_kv = shifted(term_kv.astype(jnp.bfloat16), "ctx", -distance).astype(jnp.float32)
        kv_sum = term_kv if kv_sum is None else kv_sum + term_kv
    query_grad = (
        (dq_acc * scale_factor)
        .astype(jnp.bfloat16)
        .reshape(1, tok_rows, kv_heads * group_size * HD)
    )
    kv_grad = kv_sum.astype(jnp.bfloat16)
    inner = lax.axis_size("sz")
    outer = lax.axis_size("sx")
    row_index = lax.axis_index("sx")
    col_index = lax.axis_index("sz")
    piece_count = tok_rows // PIECE
    route_table = route[0]
    seq_count = route_table.shape[0]
    piece_rows = kv_grad.reshape(piece_count, PIECE, kv_heads, 2 * HD)
    my_route = lax.dynamic_index_in_dim(route_table, row_index * inner + col_index, 0, keepdims=False)
    col_ids = jnp.arange(inner, dtype=jnp.int32)
    to_col = (my_route[None, :] % inner == col_ids[:, None]).astype(jnp.bfloat16)
    first_out = jnp.einsum(
        "cp,pxhw->cpxhw", to_col, piece_rows, preferred_element_type=jnp.bfloat16
    )
    first_in = lax.all_to_all(first_out, "sz", split_axis=0, concat_axis=0, tiled=True)
    row_routes = lax.dynamic_slice_in_dim(route_table, row_index * inner, inner, 0)
    owners = jnp.arange(seq_count, dtype=jnp.int32)
    hits = (route_table[:, :, None] == owners[None, None, :]).astype(jnp.int32)
    sends = jnp.sum(hits, 1)
    ranks = jnp.cumsum(sends, 0) - sends
    row_ranks = lax.dynamic_slice_in_dim(ranks, row_index * inner, inner, 0)
    slot_ids = jnp.arange(2 * piece_count, dtype=jnp.int32)
    target_rows = jnp.arange(outer, dtype=jnp.int32)
    target_owner = target_rows * inner + col_index
    piece_owner = row_routes
    piece_rank = jnp.take_along_axis(row_ranks, piece_owner, axis=1)
    second_map = (
        (piece_owner[None, None, :, :] == target_owner[:, None, None, None])
        & (piece_rank[None, None, :, :] == slot_ids[None, :, None, None])
    ).astype(jnp.bfloat16)
    second_out = jnp.einsum(
        "tkzp,zpxhw->tkxhw", second_map, first_in, preferred_element_type=jnp.float32
    ).astype(jnp.bfloat16)
    second_in = lax.all_to_all(second_out, "sx", split_axis=0, concat_axis=0, tiled=True)
    owned = jnp.sum(second_in.astype(jnp.float32), 0).astype(jnp.bfloat16)
    return (query_grad, owned.reshape(1, 2 * piece_count * PIECE, kv_heads, 2 * HD))


def solution(mesh):
    seq_count = mesh.shape["seq"]
    inner = 8 if seq_count % 8 == 0 else 1
    split_mesh = Mesh(
        mesh.devices.reshape(mesh.shape["ctx"], seq_count // inner, inner, mesh.shape["head"]),
        ("ctx", "sx", "sz", "head"),
    )
    seq = ("sx", "sz")
    placed = (
        P(seq, "ctx", "head"),
        P(seq, "ctx", "head", None),
        P(seq, "ctx", "head"),
        P(seq, None),
        P("ctx", None, None),
    )
    return jax.shard_map(
        shards,
        mesh=split_mesh,
        in_specs=placed,
        out_specs=(P(seq, "ctx", "head"), P(seq, "ctx", "head", None)),
        check_vma=False,
    )
```

```python
import functools

import jax
import jax.numpy as jnp
from jax import lax
from jax.sharding import Mesh, PartitionSpec as P

HD = 128
PIECE = 64


def shifted(shard, axis, by):
    peers = lax.axis_size(axis)
    pairs = [(i, i + by) for i in range(peers) if 0 <= i + by < peers]
    return lax.ppermute(shard, axis, pairs)


def moved(shard, axis, pairs):
    if not pairs:
        return jnp.zeros_like(shard)
    return lax.ppermute(shard, axis, pairs)


def shards(near, queries, keys_values, out_grad, doc_ids, route):
    tok_rows = queries.shape[1]
    kv_heads = keys_values.shape[2]
    group_size = queries.shape[2] // HD // kv_heads
    ctx_index = lax.axis_index("ctx")
    reach_steps = min(3, lax.axis_size("ctx"))
    scale_factor = HD ** (-0.5)
    query_four = queries[0].reshape(tok_rows, kv_heads, group_size, HD)
    grad_four = out_grad[0].reshape(tok_rows, kv_heads, group_size, HD)
    kv_local = keys_values[0]
    doc_row = doc_ids[0]
    offsets = jnp.arange(tok_rows, dtype=jnp.int32)
    query_pos = ctx_index * tok_rows + offsets
    query_doc = lax.dynamic_slice_in_dim(doc_row, ctx_index * tok_rows, tok_rows, 0)
    blocks = lax.axis_size("ctx")
    kv_blocks = [kv_local]
    if reach_steps > 1:
        kv_blocks.append(shifted(kv_local, "ctx", 1))
    if reach_steps > 2:
        relay = [(d - 1, d) for d in range(2, blocks) if near[d - 1][d] and not near[d - 2][d - 1]]
        direct = [(d - 2, d) for d in range(2, blocks) if (d - 1, d) not in relay]
        kv_blocks.append(moved(kv_local, "ctx", direct) + moved(kv_blocks[1], "ctx", relay))
    totals = jnp.zeros((kv_heads, group_size, tok_rows), jnp.float32)
    out_acc = jnp.zeros((tok_rows, kv_heads, group_size, HD), jnp.float32)
    saved_exp = []
    for distance in range(reach_steps):
        scores = (
            jnp.einsum(
                "igad,jgd->gaij",
                query_four,
                kv_blocks[distance][..., :HD],
                preferred_element_type=jnp.float32,
            )
            * scale_factor
        )
        source = ctx_index - distance
        key_pos = source * tok_rows + offsets
        key_doc = lax.dynamic_slice_in_dim(doc_row, jnp.maximum(source, 0) * tok_rows, tok_rows, 0)
        exp_scores = jnp.where(
            (
                (query_doc[:, None] == key_doc[None, :])
                & (key_pos[None, :] <= query_pos[:, None])
                & (key_pos[None, :] >= 0)
            )[None, None],
            jnp.exp(scores),
            0.0,
        )
        saved_exp.append(exp_scores)
        totals = totals + jnp.sum(exp_scores, -1)
        out_acc = out_acc + jnp.einsum(
            "gaij,jgd->igad",
            exp_scores.astype(jnp.bfloat16),
            kv_blocks[distance][..., HD:],
            preferred_element_type=jnp.float32,
        )
    attended = out_acc / jnp.transpose(totals, (2, 0, 1))[..., None]
    delta = jnp.transpose(jnp.sum(grad_four.astype(jnp.float32) * attended, -1), (1, 2, 0))
    dq_acc = jnp.zeros((tok_rows, kv_heads, group_size, HD), jnp.float32)
    terms = []
    for distance in range(reach_steps):
        key_block = kv_blocks[distance][..., :HD]
        value_block = kv_blocks[distance][..., HD:]
        probs = saved_exp[distance] / totals[..., None]
        probs_low = probs.astype(jnp.bfloat16)
        grad_probs = jnp.einsum(
            "igad,jgd->gaij", grad_four, value_block, preferred_element_type=jnp.float32
        )
        score_low = (probs * (grad_probs - delta[..., None])).astype(jnp.bfloat16)
        dq_acc = dq_acc + jnp.einsum(
            "gaij,jgd->igad", score_low, key_block, preferred_element_type=jnp.float32
        )
        key_grad = (
            jnp.einsum("gaij,igad->jgd", score_low, query_four, preferred_element_type=jnp.float32)
            * scale_factor
        )
        value_grad = jnp.einsum(
            "gaij,igad->jgd", probs_low, grad_four, preferred_element_type=jnp.float32
        )
        terms.append(jnp.concatenate([key_grad, value_grad], -1))
    kv_sum = terms[0]
    if reach_steps == 2:
        kv_sum = kv_sum + shifted(terms[1].astype(jnp.bfloat16), "ctx", -1).astype(jnp.float32)
    elif reach_steps > 2:
        ahead = [(b + 1, b + 2) for b in range(blocks - 2) if not near[b + 1][b] and near[b + 1][b + 2]]
        back_one = [(b + 1, b) for b in range(blocks - 1) if (b + 1, b + 2) not in ahead]
        back_two = [(b + 2, b) for b in range(blocks - 2)]
        folded = terms[2] + moved(terms[1], "ctx", ahead)
        kv_sum = (
            kv_sum
            + moved(terms[1].astype(jnp.bfloat16), "ctx", back_one).astype(jnp.float32)
            + moved(folded.astype(jnp.bfloat16), "ctx", back_two).astype(jnp.float32)
        )
    query_grad = (
        (dq_acc * scale_factor)
        .astype(jnp.bfloat16)
        .reshape(1, tok_rows, kv_heads * group_size * HD)
    )
    kv_grad = kv_sum.astype(jnp.bfloat16)
    inner = lax.axis_size("sz")
    outer = lax.axis_size("sx")
    row_index = lax.axis_index("sx")
    col_index = lax.axis_index("sz")
    piece_count = tok_rows // PIECE
    route_table = route[0]
    seq_count = route_table.shape[0]
    piece_rows = kv_grad.reshape(piece_count, PIECE, kv_heads, 2 * HD)
    my_route = lax.dynamic_index_in_dim(route_table, row_index * inner + col_index, 0, keepdims=False)
    col_ids = jnp.arange(inner, dtype=jnp.int32)
    to_col = (my_route[None, :] % inner == col_ids[:, None]).astype(jnp.bfloat16)
    first_out = jnp.einsum(
        "cp,pxhw->cpxhw", to_col, piece_rows, preferred_element_type=jnp.bfloat16
    )
    first_in = lax.all_to_all(first_out, "sz", split_axis=0, concat_axis=0, tiled=True)
    row_routes = lax.dynamic_slice_in_dim(route_table, row_index * inner, inner, 0)
    owners = jnp.arange(seq_count, dtype=jnp.int32)
    hits = (route_table[:, :, None] == owners[None, None, :]).astype(jnp.int32)
    sends = jnp.sum(hits, 1)
    ranks = jnp.cumsum(sends, 0) - sends
    row_ranks = lax.dynamic_slice_in_dim(ranks, row_index * inner, inner, 0)
    slot_ids = jnp.arange(2 * piece_count, dtype=jnp.int32)
    target_rows = jnp.arange(outer, dtype=jnp.int32)
    target_owner = target_rows * inner + col_index
    piece_owner = row_routes
    piece_rank = jnp.take_along_axis(row_ranks, piece_owner, axis=1)
    second_map = (
        (piece_owner[None, None, :, :] == target_owner[:, None, None, None])
        & (piece_rank[None, None, :, :] == slot_ids[None, :, None, None])
    ).astype(jnp.bfloat16)
    second_out = jnp.einsum(
        "tkzp,zpxhw->tkxhw", second_map, first_in, preferred_element_type=jnp.float32
    ).astype(jnp.bfloat16)
    second_in = lax.all_to_all(second_out, "sx", split_axis=0, concat_axis=0, tiled=True)
    owned = jnp.sum(second_in.astype(jnp.float32), 0).astype(jnp.bfloat16)
    return (query_grad, owned.reshape(1, 2 * piece_count * PIECE, kv_heads, 2 * HD))


def solution(mesh):
    seq_count = mesh.shape["seq"]
    inner = 8 if seq_count % 8 == 0 else 1
    split_mesh = Mesh(
        mesh.devices.reshape(mesh.shape["ctx"], seq_count // inner, inner, mesh.shape["head"]),
        ("ctx", "sx", "sz", "head"),
    )
    seq = ("sx", "sz")
    placed = (
        P(seq, "ctx", "head"),
        P(seq, "ctx", "head", None),
        P(seq, "ctx", "head"),
        P(seq, None),
        P("ctx", None, None),
    )
    ctx_count = mesh.shape["ctx"]
    heights = [mesh.devices[c, 0, 0].coords[2] for c in range(ctx_count)]
    near = [[heights[a] == heights[b] for b in range(ctx_count)] for a in range(ctx_count)]
    return jax.shard_map(
        functools.partial(shards, near),
        mesh=split_mesh,
        in_specs=placed,
        out_specs=(P(seq, "ctx", "head"), P(seq, "ctx", "head", None)),
        check_vma=False,
    )
```

```python
import functools

import jax
import jax.numpy as jnp
from jax import lax
from jax.sharding import Mesh, PartitionSpec as P

HD = 128
PIECE = 64


def shifted(shard, axis, by):
    peers = lax.axis_size(axis)
    pairs = [(i, i + by) for i in range(peers) if 0 <= i + by < peers]
    return lax.ppermute(shard, axis, pairs)


def moved(shard, axis, pairs):
    if not pairs:
        return jnp.zeros_like(shard)
    return lax.ppermute(shard, axis, pairs)


def shards(near, column_mate, queries, keys_values, out_grad, doc_ids, route):
    tok_rows = queries.shape[1]
    kv_heads = keys_values.shape[2]
    group_size = queries.shape[2] // HD // kv_heads
    ctx_index = lax.axis_index("ctx")
    reach_steps = min(3, lax.axis_size("ctx"))
    scale_factor = HD ** (-0.5)
    query_four = queries[0].reshape(tok_rows, kv_heads, group_size, HD)
    grad_four = out_grad[0].reshape(tok_rows, kv_heads, group_size, HD)
    kv_local = keys_values[0]
    doc_row = doc_ids[0]
    offsets = jnp.arange(tok_rows, dtype=jnp.int32)
    query_pos = ctx_index * tok_rows + offsets
    query_doc = lax.dynamic_slice_in_dim(doc_row, ctx_index * tok_rows, tok_rows, 0)
    blocks = lax.axis_size("ctx")
    kv_blocks = [kv_local]
    if reach_steps > 1:
        kv_blocks.append(shifted(kv_local, "ctx", 1))
    if reach_steps > 2:
        relay = [(d - 1, d) for d in range(2, blocks) if near[d - 1][d] and not near[d - 2][d - 1]]
        over = [(d - 2, m) for d in range(2, blocks) for m in [column_mate[d - 2][d]]
                if (d - 1, d) not in relay and not near[d - 2][d] and m is not None]
        down = [(m, d) for d in range(2, blocks) for m in [column_mate[d - 2][d]]
                if (d - 1, d) not in relay and not near[d - 2][d] and m is not None]
        direct = [(d - 2, d) for d in range(2, blocks) if (d - 1, d) not in relay and (d - 2, d) not in
                  [(a, b) for (a, _), (_, b) in zip(over, down)]]
        kv_blocks.append(
            moved(kv_local, "ctx", direct)
            + moved(kv_blocks[1], "ctx", relay)
            + moved(moved(kv_local, "ctx", over), "ctx", down)
        )
    totals = jnp.zeros((kv_heads, group_size, tok_rows), jnp.float32)
    out_acc = jnp.zeros((tok_rows, kv_heads, group_size, HD), jnp.float32)
    saved_exp = []
    for distance in range(reach_steps):
        scores = (
            jnp.einsum(
                "igad,jgd->gaij",
                query_four,
                kv_blocks[distance][..., :HD],
                preferred_element_type=jnp.float32,
            )
            * scale_factor
        )
        source = ctx_index - distance
        key_pos = source * tok_rows + offsets
        key_doc = lax.dynamic_slice_in_dim(doc_row, jnp.maximum(source, 0) * tok_rows, tok_rows, 0)
        exp_scores = jnp.where(
            (
                (query_doc[:, None] == key_doc[None, :])
                & (key_pos[None, :] <= query_pos[:, None])
                & (key_pos[None, :] >= 0)
            )[None, None],
            jnp.exp(scores),
            0.0,
        )
        saved_exp.append(exp_scores)
        totals = totals + jnp.sum(exp_scores, -1)
        out_acc = out_acc + jnp.einsum(
            "gaij,jgd->igad",
            exp_scores.astype(jnp.bfloat16),
            kv_blocks[distance][..., HD:],
            preferred_element_type=jnp.float32,
        )
    attended = out_acc / jnp.transpose(totals, (2, 0, 1))[..., None]
    delta = jnp.transpose(jnp.sum(grad_four.astype(jnp.float32) * attended, -1), (1, 2, 0))
    dq_acc = jnp.zeros((tok_rows, kv_heads, group_size, HD), jnp.float32)
    terms = []
    for distance in range(reach_steps):
        key_block = kv_blocks[distance][..., :HD]
        value_block = kv_blocks[distance][..., HD:]
        probs = saved_exp[distance] / totals[..., None]
        probs_low = probs.astype(jnp.bfloat16)
        grad_probs = jnp.einsum(
            "igad,jgd->gaij", grad_four, value_block, preferred_element_type=jnp.float32
        )
        score_low = (probs * (grad_probs - delta[..., None])).astype(jnp.bfloat16)
        dq_acc = dq_acc + jnp.einsum(
            "gaij,jgd->igad", score_low, key_block, preferred_element_type=jnp.float32
        )
        key_grad = (
            jnp.einsum("gaij,igad->jgd", score_low, query_four, preferred_element_type=jnp.float32)
            * scale_factor
        )
        value_grad = jnp.einsum(
            "gaij,igad->jgd", probs_low, grad_four, preferred_element_type=jnp.float32
        )
        terms.append(jnp.concatenate([key_grad, value_grad], -1))
    kv_sum = terms[0]
    if reach_steps == 2:
        kv_sum = kv_sum + shifted(terms[1].astype(jnp.bfloat16), "ctx", -1).astype(jnp.float32)
    elif reach_steps > 2:
        ahead = [(b + 1, b + 2) for b in range(blocks - 2) if not near[b + 1][b] and near[b + 1][b + 2]]
        back_one = [(b + 1, b) for b in range(blocks - 1) if (b + 1, b + 2) not in ahead]
        back_two = [(b + 2, b) for b in range(blocks - 2)]
        folded = terms[2] + moved(terms[1], "ctx", ahead)
        kv_sum = (
            kv_sum
            + moved(terms[1].astype(jnp.bfloat16), "ctx", back_one).astype(jnp.float32)
            + moved(folded.astype(jnp.bfloat16), "ctx", back_two).astype(jnp.float32)
        )
    query_grad = (
        (dq_acc * scale_factor)
        .astype(jnp.bfloat16)
        .reshape(1, tok_rows, kv_heads * group_size * HD)
    )
    kv_grad = kv_sum.astype(jnp.bfloat16)
    inner = lax.axis_size("sz")
    outer = lax.axis_size("sx")
    row_index = lax.axis_index("sx")
    col_index = lax.axis_index("sz")
    piece_count = tok_rows // PIECE
    route_table = route[0]
    seq_count = route_table.shape[0]
    piece_rows = kv_grad.reshape(piece_count, PIECE, kv_heads, 2 * HD)
    my_route = lax.dynamic_index_in_dim(route_table, row_index * inner + col_index, 0, keepdims=False)
    col_ids = jnp.arange(inner, dtype=jnp.int32)
    to_col = (my_route[None, :] % inner == col_ids[:, None]).astype(jnp.bfloat16)
    first_out = jnp.einsum(
        "cp,pxhw->cpxhw", to_col, piece_rows, preferred_element_type=jnp.bfloat16
    )
    first_in = lax.all_to_all(first_out, "sz", split_axis=0, concat_axis=0, tiled=True)
    row_routes = lax.dynamic_slice_in_dim(route_table, row_index * inner, inner, 0)
    owners = jnp.arange(seq_count, dtype=jnp.int32)
    hits = (route_table[:, :, None] == owners[None, None, :]).astype(jnp.int32)
    sends = jnp.sum(hits, 1)
    ranks = jnp.cumsum(sends, 0) - sends
    row_ranks = lax.dynamic_slice_in_dim(ranks, row_index * inner, inner, 0)
    slot_ids = jnp.arange(2 * piece_count, dtype=jnp.int32)
    target_rows = jnp.arange(outer, dtype=jnp.int32)
    target_owner = target_rows * inner + col_index
    piece_owner = row_routes
    piece_rank = jnp.take_along_axis(row_ranks, piece_owner, axis=1)
    second_map = (
        (piece_owner[None, None, :, :] == target_owner[:, None, None, None])
        & (piece_rank[None, None, :, :] == slot_ids[None, :, None, None])
    ).astype(jnp.bfloat16)
    second_out = jnp.einsum(
        "tkzp,zpxhw->tkxhw", second_map, first_in, preferred_element_type=jnp.float32
    ).astype(jnp.bfloat16)
    second_in = lax.all_to_all(second_out, "sx", split_axis=0, concat_axis=0, tiled=True)
    owned = jnp.sum(second_in.astype(jnp.float32), 0).astype(jnp.bfloat16)
    return (query_grad, owned.reshape(1, 2 * piece_count * PIECE, kv_heads, 2 * HD))


def solution(mesh):
    seq_count = mesh.shape["seq"]
    inner = 8 if seq_count % 8 == 0 else 1
    split_mesh = Mesh(
        mesh.devices.reshape(mesh.shape["ctx"], seq_count // inner, inner, mesh.shape["head"]),
        ("ctx", "sx", "sz", "head"),
    )
    seq = ("sx", "sz")
    placed = (
        P(seq, "ctx", "head"),
        P(seq, "ctx", "head", None),
        P(seq, "ctx", "head"),
        P(seq, None),
        P("ctx", None, None),
    )
    ctx_count = mesh.shape["ctx"]
    heights = [mesh.devices[c, 0, 0].coords[2] for c in range(ctx_count)]
    near = [[heights[a] == heights[b] for b in range(ctx_count)] for a in range(ctx_count)]
    places = [tuple(mesh.devices[c, 0, 0].coords) for c in range(ctx_count)]
    column_mate = [
        [
            next((m for m in range(ctx_count) if m != b and places[m][1] == places[a][1]
                  and places[m][2] == places[b][2]), None)
            for b in range(ctx_count)
        ]
        for a in range(ctx_count)
    ]
    return jax.shard_map(
        functools.partial(shards, near, column_mate),
        mesh=split_mesh,
        in_specs=placed,
        out_specs=(P(seq, "ctx", "head"), P(seq, "ctx", "head", None)),
        check_vma=False,
    )
```

```python
import functools

import jax
import jax.numpy as jnp
from jax import lax
from jax.sharding import Mesh, PartitionSpec as P

HD = 128
PIECE = 64


def shifted(shard, axis, by):
    peers = lax.axis_size(axis)
    pairs = [(i, i + by) for i in range(peers) if 0 <= i + by < peers]
    return lax.ppermute(shard, axis, pairs)


def moved(shard, axis, pairs):
    if not pairs:
        return jnp.zeros_like(shard)
    return lax.ppermute(shard, axis, pairs)


def shards(near, queries, keys_values, out_grad, doc_ids, route):
    tok_rows = queries.shape[1]
    kv_heads = keys_values.shape[2]
    group_size = queries.shape[2] // HD // kv_heads
    ctx_index = lax.axis_index("ctx")
    reach_steps = min(3, lax.axis_size("ctx"))
    scale_factor = HD ** (-0.5)
    query_four = queries[0].reshape(tok_rows, kv_heads, group_size, HD)
    grad_four = out_grad[0].reshape(tok_rows, kv_heads, group_size, HD)
    kv_local = keys_values[0]
    doc_row = doc_ids[0]
    offsets = jnp.arange(tok_rows, dtype=jnp.int32)
    query_pos = ctx_index * tok_rows + offsets
    query_doc = lax.dynamic_slice_in_dim(doc_row, ctx_index * tok_rows, tok_rows, 0)
    blocks = lax.axis_size("ctx")
    kv_blocks = [kv_local]
    if reach_steps > 1:
        kv_blocks.append(shifted(kv_local, "ctx", 1))
    if reach_steps > 2:
        relay = [(d - 1, d) for d in range(2, blocks) if near[d - 1][d] and not near[d - 2][d - 1]]
        direct = [(d - 2, d) for d in range(2, blocks) if (d - 1, d) not in relay]
        kv_blocks.append(moved(kv_local, "ctx", direct) + moved(kv_blocks[1], "ctx", relay))
    window = jnp.concatenate(kv_blocks, 0)
    key_window = window[..., :HD]
    value_window = window[..., HD:]
    seen_parts = []
    for distance in range(reach_steps):
        source = ctx_index - distance
        key_pos = source * tok_rows + offsets
        key_doc = lax.dynamic_slice_in_dim(doc_row, jnp.maximum(source, 0) * tok_rows, tok_rows, 0)
        seen_parts.append(
            (query_doc[:, None] == key_doc[None, :])
            & (key_pos[None, :] <= query_pos[:, None])
            & (key_pos[None, :] >= 0)
        )
    seen = jnp.concatenate(seen_parts, 1)
    scores = (
        jnp.einsum("igad,jgd->gaij", query_four, key_window, preferred_element_type=jnp.float32)
        * scale_factor
    )
    exp_scores = jnp.where(seen[None, None], jnp.exp(scores), 0.0)
    totals = jnp.sum(exp_scores, -1)
    out_acc = jnp.einsum(
        "gaij,jgd->igad",
        exp_scores.astype(jnp.bfloat16),
        value_window,
        preferred_element_type=jnp.float32,
    )
    attended = out_acc / jnp.transpose(totals, (2, 0, 1))[..., None]
    delta = jnp.transpose(jnp.sum(grad_four.astype(jnp.float32) * attended, -1), (1, 2, 0))
    probs = exp_scores / totals[..., None]
    probs_low = probs.astype(jnp.bfloat16)
    grad_probs = jnp.einsum(
        "igad,jgd->gaij", grad_four, value_window, preferred_element_type=jnp.float32
    )
    score_low = (probs * (grad_probs - delta[..., None])).astype(jnp.bfloat16)
    dq_acc = jnp.einsum(
        "gaij,jgd->igad", score_low, key_window, preferred_element_type=jnp.float32
    )
    key_grad = (
        jnp.einsum("gaij,igad->jgd", score_low, query_four, preferred_element_type=jnp.float32)
        * scale_factor
    )
    value_grad = jnp.einsum(
        "gaij,igad->jgd", probs_low, grad_four, preferred_element_type=jnp.float32
    )
    both = jnp.concatenate([key_grad, value_grad], -1)
    terms = [both[d * tok_rows:(d + 1) * tok_rows] for d in range(reach_steps)]
    kv_sum = terms[0]
    if reach_steps == 2:
        kv_sum = kv_sum + shifted(terms[1].astype(jnp.bfloat16), "ctx", -1).astype(jnp.float32)
    elif reach_steps > 2:
        ahead = [(b + 1, b + 2) for b in range(blocks - 2) if not near[b + 1][b] and near[b + 1][b + 2]]
        back_one = [(b + 1, b) for b in range(blocks - 1) if (b + 1, b + 2) not in ahead]
        back_two = [(b + 2, b) for b in range(blocks - 2)]
        folded = terms[2] + moved(terms[1], "ctx", ahead)
        kv_sum = (
            kv_sum
            + moved(terms[1].astype(jnp.bfloat16), "ctx", back_one).astype(jnp.float32)
            + moved(folded.astype(jnp.bfloat16), "ctx", back_two).astype(jnp.float32)
        )
    query_grad = (
        (dq_acc * scale_factor)
        .astype(jnp.bfloat16)
        .reshape(1, tok_rows, kv_heads * group_size * HD)
    )
    kv_grad = kv_sum.astype(jnp.bfloat16)
    inner = lax.axis_size("sz")
    outer = lax.axis_size("sx")
    row_index = lax.axis_index("sx")
    col_index = lax.axis_index("sz")
    piece_count = tok_rows // PIECE
    route_table = route[0]
    seq_count = route_table.shape[0]
    piece_rows = kv_grad.reshape(piece_count, PIECE, kv_heads, 2 * HD)
    my_route = lax.dynamic_index_in_dim(route_table, row_index * inner + col_index, 0, keepdims=False)
    col_ids = jnp.arange(inner, dtype=jnp.int32)
    to_col = (my_route[None, :] % inner == col_ids[:, None]).astype(jnp.bfloat16)
    first_out = jnp.einsum(
        "cp,pxhw->cpxhw", to_col, piece_rows, preferred_element_type=jnp.bfloat16
    )
    first_in = lax.all_to_all(first_out, "sz", split_axis=0, concat_axis=0, tiled=True)
    row_routes = lax.dynamic_slice_in_dim(route_table, row_index * inner, inner, 0)
    owners = jnp.arange(seq_count, dtype=jnp.int32)
    hits = (route_table[:, :, None] == owners[None, None, :]).astype(jnp.int32)
    sends = jnp.sum(hits, 1)
    ranks = jnp.cumsum(sends, 0) - sends
    row_ranks = lax.dynamic_slice_in_dim(ranks, row_index * inner, inner, 0)
    slot_ids = jnp.arange(2 * piece_count, dtype=jnp.int32)
    target_rows = jnp.arange(outer, dtype=jnp.int32)
    target_owner = target_rows * inner + col_index
    piece_owner = row_routes
    piece_rank = jnp.take_along_axis(row_ranks, piece_owner, axis=1)
    second_map = (
        (piece_owner[None, None, :, :] == target_owner[:, None, None, None])
        & (piece_rank[None, None, :, :] == slot_ids[None, :, None, None])
    ).astype(jnp.bfloat16)
    second_out = jnp.einsum(
        "tkzp,zpxhw->tkxhw", second_map, first_in, preferred_element_type=jnp.float32
    ).astype(jnp.bfloat16)
    second_in = lax.all_to_all(second_out, "sx", split_axis=0, concat_axis=0, tiled=True)
    owned = jnp.sum(second_in.astype(jnp.float32), 0).astype(jnp.bfloat16)
    return (query_grad, owned.reshape(1, 2 * piece_count * PIECE, kv_heads, 2 * HD))


def solution(mesh):
    seq_count = mesh.shape["seq"]
    inner = 8 if seq_count % 8 == 0 else 1
    split_mesh = Mesh(
        mesh.devices.reshape(mesh.shape["ctx"], seq_count // inner, inner, mesh.shape["head"]),
        ("ctx", "sx", "sz", "head"),
    )
    seq = ("sx", "sz")
    placed = (
        P(seq, "ctx", "head"),
        P(seq, "ctx", "head", None),
        P(seq, "ctx", "head"),
        P(seq, None),
        P("ctx", None, None),
    )
    ctx_count = mesh.shape["ctx"]
    heights = [mesh.devices[c, 0, 0].coords[2] for c in range(ctx_count)]
    near = [[heights[a] == heights[b] for b in range(ctx_count)] for a in range(ctx_count)]
    return jax.shard_map(
        functools.partial(shards, near),
        mesh=split_mesh,
        in_specs=placed,
        out_specs=(P(seq, "ctx", "head"), P(seq, "ctx", "head", None)),
        check_vma=False,
    )
```

```python
import functools

import jax
import jax.numpy as jnp
from jax import lax
from jax.sharding import Mesh, PartitionSpec as P

HD = 128
PIECE = 64


def shifted(shard, axis, by):
    peers = lax.axis_size(axis)
    pairs = [(i, i + by) for i in range(peers) if 0 <= i + by < peers]
    return lax.ppermute(shard, axis, pairs)


def moved(shard, axis, pairs):
    if not pairs:
        return jnp.zeros_like(shard)
    return lax.ppermute(shard, axis, pairs)


def shards(near, queries, keys_values, out_grad, doc_ids, route):
    tok_rows = queries.shape[1]
    kv_heads = keys_values.shape[2]
    group_size = queries.shape[2] // HD // kv_heads
    ctx_index = lax.axis_index("ctx")
    reach_steps = min(3, lax.axis_size("ctx"))
    scale_factor = HD ** (-0.5)
    query_four = queries[0].reshape(tok_rows, kv_heads, group_size, HD)
    grad_four = out_grad[0].reshape(tok_rows, kv_heads, group_size, HD)
    kv_local = keys_values[0]
    doc_row = doc_ids[0]
    offsets = jnp.arange(tok_rows, dtype=jnp.int32)
    query_pos = ctx_index * tok_rows + offsets
    query_doc = lax.dynamic_slice_in_dim(doc_row, ctx_index * tok_rows, tok_rows, 0)
    blocks = lax.axis_size("ctx")
    kv_blocks = [kv_local]
    if reach_steps > 1:
        kv_blocks.append(shifted(kv_local, "ctx", 1))
    if reach_steps > 2:
        relay = [(d - 1, d) for d in range(2, blocks) if near[d - 1][d] and not near[d - 2][d - 1]]
        direct = [(d - 2, d) for d in range(2, blocks) if (d - 1, d) not in relay]
        kv_blocks.append(moved(kv_local, "ctx", direct) + moved(kv_blocks[1], "ctx", relay))
    window = jnp.concatenate(kv_blocks, 0)
    key_window = window[..., :HD]
    value_window = window[..., HD:]
    seen_parts = []
    for distance in range(reach_steps):
        source = ctx_index - distance
        key_pos = source * tok_rows + offsets
        key_doc = lax.dynamic_slice_in_dim(doc_row, jnp.maximum(source, 0) * tok_rows, tok_rows, 0)
        seen_parts.append(
            (query_doc[:, None] == key_doc[None, :])
            & (key_pos[None, :] <= query_pos[:, None])
            & (key_pos[None, :] >= 0)
        )
    seen = jnp.concatenate(seen_parts, 1)
    scores = (
        jnp.einsum("igad,jgd->gaij", query_four, key_window, preferred_element_type=jnp.float32)
        * scale_factor
    )
    exp_scores = jnp.where(seen[None, None], jnp.exp(scores), 0.0)
    totals = jnp.sum(exp_scores, -1)
    out_acc = jnp.einsum(
        "gaij,jgd->igad",
        exp_scores.astype(jnp.bfloat16),
        value_window,
        preferred_element_type=jnp.float32,
    )
    attended = out_acc / jnp.transpose(totals, (2, 0, 1))[..., None]
    delta = jnp.transpose(jnp.sum(grad_four.astype(jnp.float32) * attended, -1), (1, 2, 0))
    probs = exp_scores / totals[..., None]
    probs_low = probs.astype(jnp.bfloat16)
    grad_probs = jnp.einsum(
        "igad,jgd->gaij", grad_four, value_window, preferred_element_type=jnp.float32
    )
    score_low = (probs * (grad_probs - delta[..., None])).astype(jnp.bfloat16)
    dq_acc = jnp.einsum(
        "gaij,jgd->igad", score_low, key_window, preferred_element_type=jnp.float32
    )
    key_grad = (
        jnp.einsum("gaij,igad->jgd", score_low, query_four, preferred_element_type=jnp.float32)
        * scale_factor
    )
    value_grad = jnp.einsum(
        "gaij,igad->jgd", probs_low, grad_four, preferred_element_type=jnp.float32
    )
    both = jnp.concatenate([key_grad, value_grad], -1)
    terms = [both[d * tok_rows:(d + 1) * tok_rows] for d in range(reach_steps)]
    kv_sum = terms[0]
    if reach_steps == 2:
        kv_sum = kv_sum + shifted(terms[1].astype(jnp.bfloat16), "ctx", -1).astype(jnp.float32)
    elif reach_steps > 2:
        ahead = [(b + 1, b + 2) for b in range(blocks - 2) if not near[b + 1][b] and near[b + 1][b + 2]]
        back_one = [(b + 1, b) for b in range(blocks - 1) if (b + 1, b + 2) not in ahead]
        back_two = [(b + 2, b) for b in range(blocks - 2)]
        folded = terms[2] + moved(terms[1], "ctx", ahead)
        kv_sum = (
            kv_sum
            + moved(terms[1].astype(jnp.bfloat16), "ctx", back_one).astype(jnp.float32)
            + moved(folded.astype(jnp.bfloat16), "ctx", back_two).astype(jnp.float32)
        )
    query_grad = (
        (dq_acc * scale_factor)
        .astype(jnp.bfloat16)
        .reshape(1, tok_rows, kv_heads * group_size * HD)
    )
    kv_grad = kv_sum.astype(jnp.bfloat16)
    inner = lax.axis_size("sz")
    outer = lax.axis_size("sx")
    row_index = lax.axis_index("sx")
    col_index = lax.axis_index("sz")
    piece_count = tok_rows // PIECE
    route_table = route[0]
    seq_count = route_table.shape[0]
    piece_rows = kv_grad.reshape(piece_count, PIECE, kv_heads, 2 * HD)
    my_route = lax.dynamic_index_in_dim(route_table, row_index * inner + col_index, 0, keepdims=False)
    col_ids = jnp.arange(inner, dtype=jnp.int32)
    to_col = (my_route[None, :] % inner == col_ids[:, None]).astype(jnp.bfloat16)
    first_out = jnp.einsum(
        "cp,pxhw->cpxhw", to_col, piece_rows, preferred_element_type=jnp.bfloat16
    )
    first_in = lax.all_to_all(first_out, "sz", split_axis=0, concat_axis=0, tiled=True)
    row_routes = lax.dynamic_slice_in_dim(route_table, row_index * inner, inner, 0)
    owners = jnp.arange(seq_count, dtype=jnp.int32)
    hits = (route_table[:, :, None] == owners[None, None, :]).astype(jnp.int32)
    sends = jnp.sum(hits, 1)
    ranks = jnp.cumsum(sends, 0) - sends
    row_ranks = lax.dynamic_slice_in_dim(ranks, row_index * inner, inner, 0)
    slot_ids = jnp.arange(2 * piece_count, dtype=jnp.int32)
    target_rows = jnp.arange(outer, dtype=jnp.int32)
    target_owner = target_rows * inner + col_index
    piece_owner = row_routes
    piece_rank = jnp.take_along_axis(row_ranks, piece_owner, axis=1)
    second_map = (
        (piece_owner[None, None, :, :] == target_owner[:, None, None, None])
        & (piece_rank[None, None, :, :] == slot_ids[None, :, None, None])
    ).astype(jnp.bfloat16)
    second_out = jnp.einsum(
        "tkzp,zpxhw->tkxhw", second_map, first_in, preferred_element_type=jnp.float32
    ).astype(jnp.bfloat16)
    owned_sum = lax.dynamic_index_in_dim(second_out, row_index, 0, keepdims=False).astype(jnp.float32)
    for step in range(1, outer):
        outbound = lax.dynamic_index_in_dim(second_out, (row_index + step) % outer, 0, keepdims=False)
        inbound = lax.ppermute(outbound, "sx", [(i, (i + step) % outer) for i in range(outer)])
        owned_sum = owned_sum + inbound.astype(jnp.float32)
    owned = owned_sum.astype(jnp.bfloat16)
    return (query_grad, owned.reshape(1, 2 * piece_count * PIECE, kv_heads, 2 * HD))


def solution(mesh):
    seq_count = mesh.shape["seq"]
    inner = 8 if seq_count % 8 == 0 else 1
    split_mesh = Mesh(
        mesh.devices.reshape(mesh.shape["ctx"], seq_count // inner, inner, mesh.shape["head"]),
        ("ctx", "sx", "sz", "head"),
    )
    seq = ("sx", "sz")
    placed = (
        P(seq, "ctx", "head"),
        P(seq, "ctx", "head", None),
        P(seq, "ctx", "head"),
        P(seq, None),
        P("ctx", None, None),
    )
    ctx_count = mesh.shape["ctx"]
    heights = [mesh.devices[c, 0, 0].coords[2] for c in range(ctx_count)]
    near = [[heights[a] == heights[b] for b in range(ctx_count)] for a in range(ctx_count)]
    return jax.shard_map(
        functools.partial(shards, near),
        mesh=split_mesh,
        in_specs=placed,
        out_specs=(P(seq, "ctx", "head"), P(seq, "ctx", "head", None)),
        check_vma=False,
    )
```

```python
import functools

import jax
import jax.numpy as jnp
from jax import lax
from jax.sharding import Mesh, PartitionSpec as P

HD = 128
PIECE = 64


def shifted(shard, axis, by):
    peers = lax.axis_size(axis)
    pairs = [(i, i + by) for i in range(peers) if 0 <= i + by < peers]
    return lax.ppermute(shard, axis, pairs)


def moved(shard, axis, pairs):
    if not pairs:
        return jnp.zeros_like(shard)
    return lax.ppermute(shard, axis, pairs)


def shards(near, queries, keys_values, out_grad, doc_ids, route):
    tok_rows = queries.shape[1]
    kv_heads = keys_values.shape[2]
    group_size = queries.shape[2] // HD // kv_heads
    ctx_index = lax.axis_index("ctx")
    reach_steps = min(3, lax.axis_size("ctx"))
    scale_factor = HD ** (-0.5)
    query_four = queries[0].reshape(tok_rows, kv_heads, group_size, HD)
    grad_four = out_grad[0].reshape(tok_rows, kv_heads, group_size, HD)
    kv_local = keys_values[0]
    doc_row = doc_ids[0]
    offsets = jnp.arange(tok_rows, dtype=jnp.int32)
    query_pos = ctx_index * tok_rows + offsets
    query_doc = lax.dynamic_slice_in_dim(doc_row, ctx_index * tok_rows, tok_rows, 0)
    blocks = lax.axis_size("ctx")
    kv_blocks = [kv_local]
    if reach_steps > 1:
        kv_blocks.append(shifted(kv_local, "ctx", 1))
    if reach_steps > 2:
        relay = [(d - 1, d) for d in range(2, blocks) if near[d - 1][d] and not near[d - 2][d - 1]]
        direct = [(d - 2, d) for d in range(2, blocks) if (d - 1, d) not in relay]
        kv_blocks.append(moved(kv_local, "ctx", direct) + moved(kv_blocks[1], "ctx", relay))
    window = jnp.concatenate(kv_blocks, 0)
    key_window = window[..., :HD]
    value_window = window[..., HD:]
    seen_parts = []
    for distance in range(reach_steps):
        source = ctx_index - distance
        key_pos = source * tok_rows + offsets
        key_doc = lax.dynamic_slice_in_dim(doc_row, jnp.maximum(source, 0) * tok_rows, tok_rows, 0)
        seen_parts.append(
            (query_doc[:, None] == key_doc[None, :])
            & (key_pos[None, :] <= query_pos[:, None])
            & (key_pos[None, :] >= 0)
        )
    seen = jnp.concatenate(seen_parts, 1)
    own_scores = jnp.einsum(
        "igad,jgd->gaij", query_four, kv_local[..., :HD], preferred_element_type=jnp.float32
    )
    own_grad_probs = jnp.einsum(
        "igad,jgd->gaij", grad_four, kv_local[..., HD:], preferred_element_type=jnp.float32
    )
    far_window = jnp.concatenate(kv_blocks[1:], 0)
    scores = (
        jnp.concatenate(
            [
                own_scores,
                jnp.einsum(
                    "igad,jgd->gaij", query_four, far_window[..., :HD], preferred_element_type=jnp.float32
                ),
            ],
            -1,
        )
        * scale_factor
    )
    exp_scores = jnp.where(seen[None, None], jnp.exp(scores), 0.0)
    totals = jnp.sum(exp_scores, -1)
    out_acc = jnp.einsum(
        "gaij,jgd->igad",
        exp_scores.astype(jnp.bfloat16),
        value_window,
        preferred_element_type=jnp.float32,
    )
    attended = out_acc / jnp.transpose(totals, (2, 0, 1))[..., None]
    delta = jnp.transpose(jnp.sum(grad_four.astype(jnp.float32) * attended, -1), (1, 2, 0))
    probs = exp_scores / totals[..., None]
    probs_low = probs.astype(jnp.bfloat16)
    grad_probs = jnp.concatenate(
        [
            own_grad_probs,
            jnp.einsum(
                "igad,jgd->gaij", grad_four, far_window[..., HD:], preferred_element_type=jnp.float32
            ),
        ],
        -1,
    )
    score_low = (probs * (grad_probs - delta[..., None])).astype(jnp.bfloat16)
    dq_acc = jnp.einsum(
        "gaij,jgd->igad", score_low, key_window, preferred_element_type=jnp.float32
    )
    key_grad = (
        jnp.einsum("gaij,igad->jgd", score_low, query_four, preferred_element_type=jnp.float32)
        * scale_factor
    )
    value_grad = jnp.einsum(
        "gaij,igad->jgd", probs_low, grad_four, preferred_element_type=jnp.float32
    )
    both = jnp.concatenate([key_grad, value_grad], -1)
    terms = [both[d * tok_rows:(d + 1) * tok_rows] for d in range(reach_steps)]
    kv_sum = terms[0]
    if reach_steps == 2:
        kv_sum = kv_sum + shifted(terms[1].astype(jnp.bfloat16), "ctx", -1).astype(jnp.float32)
    elif reach_steps > 2:
        ahead = [(b + 1, b + 2) for b in range(blocks - 2) if not near[b + 1][b] and near[b + 1][b + 2]]
        back_one = [(b + 1, b) for b in range(blocks - 1) if (b + 1, b + 2) not in ahead]
        back_two = [(b + 2, b) for b in range(blocks - 2)]
        folded = terms[2] + moved(terms[1], "ctx", ahead)
        kv_sum = (
            kv_sum
            + moved(terms[1].astype(jnp.bfloat16), "ctx", back_one).astype(jnp.float32)
            + moved(folded.astype(jnp.bfloat16), "ctx", back_two).astype(jnp.float32)
        )
    query_grad = (
        (dq_acc * scale_factor)
        .astype(jnp.bfloat16)
        .reshape(1, tok_rows, kv_heads * group_size * HD)
    )
    kv_grad = kv_sum.astype(jnp.bfloat16)
    inner = lax.axis_size("sz")
    outer = lax.axis_size("sx")
    row_index = lax.axis_index("sx")
    col_index = lax.axis_index("sz")
    piece_count = tok_rows // PIECE
    route_table = route[0]
    seq_count = route_table.shape[0]
    piece_rows = kv_grad.reshape(piece_count, PIECE, kv_heads, 2 * HD)
    my_route = lax.dynamic_index_in_dim(route_table, row_index * inner + col_index, 0, keepdims=False)
    col_ids = jnp.arange(inner, dtype=jnp.int32)
    to_col = (my_route[None, :] % inner == col_ids[:, None]).astype(jnp.bfloat16)
    first_out = jnp.einsum(
        "cp,pxhw->cpxhw", to_col, piece_rows, preferred_element_type=jnp.bfloat16
    )
    first_in = lax.all_to_all(first_out, "sz", split_axis=0, concat_axis=0, tiled=True)
    row_routes = lax.dynamic_slice_in_dim(route_table, row_index * inner, inner, 0)
    owners = jnp.arange(seq_count, dtype=jnp.int32)
    hits = (route_table[:, :, None] == owners[None, None, :]).astype(jnp.int32)
    sends = jnp.sum(hits, 1)
    ranks = jnp.cumsum(sends, 0) - sends
    row_ranks = lax.dynamic_slice_in_dim(ranks, row_index * inner, inner, 0)
    slot_ids = jnp.arange(2 * piece_count, dtype=jnp.int32)
    target_rows = jnp.arange(outer, dtype=jnp.int32)
    target_owner = target_rows * inner + col_index
    piece_owner = row_routes
    piece_rank = jnp.take_along_axis(row_ranks, piece_owner, axis=1)
    second_map = (
        (piece_owner[None, None, :, :] == target_owner[:, None, None, None])
        & (piece_rank[None, None, :, :] == slot_ids[None, :, None, None])
    ).astype(jnp.bfloat16)
    second_out = jnp.einsum(
        "tkzp,zpxhw->tkxhw", second_map, first_in, preferred_element_type=jnp.float32
    ).astype(jnp.bfloat16)
    second_in = lax.all_to_all(second_out, "sx", split_axis=0, concat_axis=0, tiled=True)
    owned = jnp.sum(second_in.astype(jnp.float32), 0).astype(jnp.bfloat16)
    return (query_grad, owned.reshape(1, 2 * piece_count * PIECE, kv_heads, 2 * HD))


def solution(mesh):
    seq_count = mesh.shape["seq"]
    inner = 8 if seq_count % 8 == 0 else 1
    split_mesh = Mesh(
        mesh.devices.reshape(mesh.shape["ctx"], seq_count // inner, inner, mesh.shape["head"]),
        ("ctx", "sx", "sz", "head"),
    )
    seq = ("sx", "sz")
    placed = (
        P(seq, "ctx", "head"),
        P(seq, "ctx", "head", None),
        P(seq, "ctx", "head"),
        P(seq, None),
        P("ctx", None, None),
    )
    ctx_count = mesh.shape["ctx"]
    heights = [mesh.devices[c, 0, 0].coords[2] for c in range(ctx_count)]
    near = [[heights[a] == heights[b] for b in range(ctx_count)] for a in range(ctx_count)]
    return jax.shard_map(
        functools.partial(shards, near),
        mesh=split_mesh,
        in_specs=placed,
        out_specs=(P(seq, "ctx", "head"), P(seq, "ctx", "head", None)),
        check_vma=False,
    )
```

```python
import functools

import jax
import jax.numpy as jnp
from jax import lax
from jax.sharding import Mesh, PartitionSpec as P

HD = 128
PIECE = 64


def shifted(shard, axis, by):
    peers = lax.axis_size(axis)
    pairs = [(i, i + by) for i in range(peers) if 0 <= i + by < peers]
    return lax.ppermute(shard, axis, pairs)


def moved(shard, axis, pairs):
    if not pairs:
        return jnp.zeros_like(shard)
    return lax.ppermute(shard, axis, pairs)


def shards(near, queries, keys_values, out_grad, doc_ids, route):
    tok_rows = queries.shape[1]
    kv_heads = keys_values.shape[2]
    group_size = queries.shape[2] // HD // kv_heads
    ctx_index = lax.axis_index("ctx")
    reach_steps = min(3, lax.axis_size("ctx"))
    scale_factor = HD ** (-0.5)
    query_four = queries[0].reshape(tok_rows, kv_heads, group_size, HD)
    grad_four = out_grad[0].reshape(tok_rows, kv_heads, group_size, HD)
    kv_local = keys_values[0]
    doc_row = doc_ids[0]
    offsets = jnp.arange(tok_rows, dtype=jnp.int32)
    query_pos = ctx_index * tok_rows + offsets
    query_doc = lax.dynamic_slice_in_dim(doc_row, ctx_index * tok_rows, tok_rows, 0)
    blocks = lax.axis_size("ctx")
    kv_blocks = [kv_local]
    if reach_steps > 1:
        kv_blocks.append(shifted(kv_local, "ctx", 1))
    if reach_steps > 2:
        relay = [(d - 1, d) for d in range(2, blocks) if near[d - 1][d] and not near[d - 2][d - 1]]
        direct = [(d - 2, d) for d in range(2, blocks) if (d - 1, d) not in relay]
        kv_blocks.append(moved(kv_local, "ctx", direct) + moved(kv_blocks[1], "ctx", relay))
    window = jnp.concatenate(kv_blocks, 0)
    key_window = window[..., :HD]
    value_window = window[..., HD:]
    seen_parts = []
    for distance in range(reach_steps):
        source = ctx_index - distance
        key_pos = source * tok_rows + offsets
        key_doc = lax.dynamic_slice_in_dim(doc_row, jnp.maximum(source, 0) * tok_rows, tok_rows, 0)
        seen_parts.append(
            (query_doc[:, None] == key_doc[None, :])
            & (key_pos[None, :] <= query_pos[:, None])
            & (key_pos[None, :] >= 0)
        )
    seen = jnp.concatenate(seen_parts, 1)
    scores = (
        jnp.einsum("igad,jgd->gaij", query_four, key_window, preferred_element_type=jnp.float32)
        * scale_factor
    )
    exp_scores = jnp.where(seen[None, None], jnp.exp(scores), 0.0)
    totals = jnp.sum(exp_scores, -1)
    out_acc = jnp.einsum(
        "gaij,jgd->igad",
        exp_scores.astype(jnp.bfloat16),
        value_window,
        preferred_element_type=jnp.float32,
    )
    attended = out_acc / jnp.transpose(totals, (2, 0, 1))[..., None]
    delta = jnp.transpose(jnp.sum(grad_four.astype(jnp.float32) * attended, -1), (1, 2, 0))
    probs = exp_scores / totals[..., None]
    probs_low = probs.astype(jnp.bfloat16)
    grad_probs = jnp.einsum(
        "igad,jgd->gaij", grad_four, value_window, preferred_element_type=jnp.float32
    )
    score_low = (probs * (grad_probs - delta[..., None])).astype(jnp.bfloat16)
    dq_acc = jnp.einsum(
        "gaij,jgd->igad", score_low, key_window, preferred_element_type=jnp.float32
    )
    key_grad = (
        jnp.einsum("gaij,igad->jgd", score_low, query_four, preferred_element_type=jnp.float32)
        * scale_factor
    )
    value_grad = jnp.einsum(
        "gaij,igad->jgd", probs_low, grad_four, preferred_element_type=jnp.float32
    )
    both = jnp.concatenate([key_grad, value_grad], -1)
    terms = [both[d * tok_rows:(d + 1) * tok_rows] for d in range(reach_steps)]
    kv_sum = terms[0]
    if reach_steps == 2:
        kv_sum = kv_sum + shifted(terms[1].astype(jnp.bfloat16), "ctx", -1).astype(jnp.float32)
    elif reach_steps > 2:
        ahead = [(b + 1, b + 2) for b in range(blocks - 2) if not near[b + 1][b] and near[b + 1][b + 2]]
        back_one = [(b + 1, b) for b in range(blocks - 1) if (b + 1, b + 2) not in ahead]
        back_two = [(b + 2, b) for b in range(blocks - 2)]
        folded = terms[2] + moved(terms[1], "ctx", ahead)
        kv_sum = (
            kv_sum
            + moved(terms[1].astype(jnp.bfloat16), "ctx", back_one).astype(jnp.float32)
            + moved(folded.astype(jnp.bfloat16), "ctx", back_two).astype(jnp.float32)
        )
    query_grad = (
        (dq_acc * scale_factor)
        .astype(jnp.bfloat16)
        .reshape(1, tok_rows, kv_heads * group_size * HD)
    )
    kv_grad = kv_sum.astype(jnp.bfloat16)
    inner = lax.axis_size("sz")
    outer = lax.axis_size("sx")
    row_index = lax.axis_index("sx")
    col_index = lax.axis_index("sz")
    piece_count = tok_rows // PIECE
    route_table = route[0]
    seq_count = route_table.shape[0]
    piece_rows = kv_grad.reshape(piece_count, PIECE, kv_heads, 2 * HD)
    my_route = lax.dynamic_index_in_dim(route_table, row_index * inner + col_index, 0, keepdims=False)
    col_ids = jnp.arange(inner, dtype=jnp.int32)
    to_col = (my_route[None, :] % inner == col_ids[:, None]).astype(jnp.bfloat16)
    first_out = jnp.einsum(
        "cp,pxhw->cpxhw", to_col, piece_rows, preferred_element_type=jnp.bfloat16
    )
    first_in = lax.all_to_all(first_out, "sz", split_axis=0, concat_axis=0, tiled=True)
    row_routes = lax.dynamic_slice_in_dim(route_table, row_index * inner, inner, 0)
    owners = jnp.arange(seq_count, dtype=jnp.int32)
    hits = (route_table[:, :, None] == owners[None, None, :]).astype(jnp.int32)
    sends = jnp.sum(hits, 1)
    ranks = jnp.cumsum(sends, 0) - sends
    row_ranks = lax.dynamic_slice_in_dim(ranks, row_index * inner, inner, 0)
    slot_ids = jnp.arange(2 * piece_count, dtype=jnp.int32)
    target_rows = jnp.arange(outer, dtype=jnp.int32)
    target_owner = target_rows * inner + col_index
    piece_owner = row_routes
    piece_rank = jnp.take_along_axis(row_ranks, piece_owner, axis=1)
    second_map = (
        (piece_owner[None, None, :, :] == target_owner[:, None, None, None])
        & (piece_rank[None, None, :, :] == slot_ids[None, :, None, None])
    ).astype(jnp.bfloat16)
    second_out = jnp.einsum(
        "tkzp,zpxhw->tkxhw", second_map, first_in, preferred_element_type=jnp.bfloat16
    )
    second_in = lax.all_to_all(second_out, "sx", split_axis=0, concat_axis=0, tiled=True)
    owned = second_in[0]
    for source in range(1, outer):
        owned = owned + second_in[source]
    return (query_grad, owned.reshape(1, 2 * piece_count * PIECE, kv_heads, 2 * HD))


def solution(mesh):
    seq_count = mesh.shape["seq"]
    inner = 8 if seq_count % 8 == 0 else 1
    split_mesh = Mesh(
        mesh.devices.reshape(mesh.shape["ctx"], seq_count // inner, inner, mesh.shape["head"]),
        ("ctx", "sx", "sz", "head"),
    )
    seq = ("sx", "sz")
    placed = (
        P(seq, "ctx", "head"),
        P(seq, "ctx", "head", None),
        P(seq, "ctx", "head"),
        P(seq, None),
        P("ctx", None, None),
    )
    ctx_count = mesh.shape["ctx"]
    heights = [mesh.devices[c, 0, 0].coords[2] for c in range(ctx_count)]
    near = [[heights[a] == heights[b] for b in range(ctx_count)] for a in range(ctx_count)]
    return jax.shard_map(
        functools.partial(shards, near),
        mesh=split_mesh,
        in_specs=placed,
        out_specs=(P(seq, "ctx", "head"), P(seq, "ctx", "head", None)),
        check_vma=False,
    )
```

```python
import functools

import jax
import jax.numpy as jnp
from jax import lax
from jax.sharding import Mesh, PartitionSpec as P

HD = 128
PIECE = 64


def shifted(shard, axis, by):
    peers = lax.axis_size(axis)
    pairs = [(i, i + by) for i in range(peers) if 0 <= i + by < peers]
    return lax.ppermute(shard, axis, pairs)


def moved(shard, axis, pairs):
    if not pairs:
        return jnp.zeros_like(shard)
    return lax.ppermute(shard, axis, pairs)


def shards(near, queries, keys_values, out_grad, doc_ids, route):
    tok_rows = queries.shape[1]
    kv_heads = keys_values.shape[2]
    group_size = queries.shape[2] // HD // kv_heads
    ctx_index = lax.axis_index("ctx")
    reach_steps = min(3, lax.axis_size("ctx"))
    scale_factor = HD ** (-0.5)
    query_four = queries[0].reshape(tok_rows, kv_heads, group_size, HD)
    grad_four = out_grad[0].reshape(tok_rows, kv_heads, group_size, HD)
    kv_local = keys_values[0]
    doc_row = doc_ids[0]
    offsets = jnp.arange(tok_rows, dtype=jnp.int32)
    query_pos = ctx_index * tok_rows + offsets
    query_doc = lax.dynamic_slice_in_dim(doc_row, ctx_index * tok_rows, tok_rows, 0)
    blocks = lax.axis_size("ctx")
    kv_blocks = [kv_local]
    if reach_steps > 1:
        kv_blocks.append(shifted(kv_local, "ctx", 1))
    if reach_steps > 2:
        relay = [(d - 1, d) for d in range(2, blocks) if near[d - 1][d] and not near[d - 2][d - 1]]
        direct = [(d - 2, d) for d in range(2, blocks) if (d - 1, d) not in relay]
        kv_blocks.append(moved(kv_local, "ctx", direct) + moved(kv_blocks[1], "ctx", relay))
    window = jnp.concatenate(kv_blocks, 0)
    key_window = window[..., :HD]
    value_window = window[..., HD:]
    seen_parts = []
    for distance in range(reach_steps):
        source = ctx_index - distance
        key_pos = source * tok_rows + offsets
        key_doc = lax.dynamic_slice_in_dim(doc_row, jnp.maximum(source, 0) * tok_rows, tok_rows, 0)
        seen_parts.append(
            (query_doc[:, None] == key_doc[None, :])
            & (key_pos[None, :] <= query_pos[:, None])
            & (key_pos[None, :] >= 0)
        )
    seen = jnp.concatenate(seen_parts, 1)
    scores = (
        jnp.einsum("igad,jgd->gaij", query_four, key_window, preferred_element_type=jnp.float32)
        * scale_factor
    )
    exp_scores = jnp.where(seen[None, None], jnp.exp(scores), 0.0)
    totals = jnp.sum(exp_scores, -1)
    out_acc = jnp.einsum(
        "gaij,jgd->igad",
        exp_scores.astype(jnp.bfloat16),
        value_window,
        preferred_element_type=jnp.float32,
    )
    attended = out_acc / jnp.transpose(totals, (2, 0, 1))[..., None]
    delta = jnp.transpose(jnp.sum(grad_four.astype(jnp.float32) * attended, -1), (1, 2, 0))
    probs = exp_scores / totals[..., None]
    probs_low = probs.astype(jnp.bfloat16)
    grad_probs = jnp.einsum(
        "igad,jgd->gaij", grad_four, value_window, preferred_element_type=jnp.float32
    )
    score_low = (probs * (grad_probs - delta[..., None])).astype(jnp.bfloat16)
    dq_acc = jnp.einsum(
        "gaij,jgd->igad", score_low, key_window, preferred_element_type=jnp.float32
    )
    key_grad = (
        jnp.einsum("gaij,igad->jgd", score_low, query_four, preferred_element_type=jnp.float32)
        * scale_factor
    )
    value_grad = jnp.einsum(
        "gaij,igad->jgd", probs_low, grad_four, preferred_element_type=jnp.float32
    )
    both = jnp.concatenate([key_grad, value_grad], -1)
    terms = [both[d * tok_rows:(d + 1) * tok_rows] for d in range(reach_steps)]
    kv_sum = terms[0]
    if reach_steps == 2:
        kv_sum = kv_sum + shifted(terms[1].astype(jnp.bfloat16), "ctx", -1).astype(jnp.float32)
    elif reach_steps > 2:
        ahead = [(b + 1, b + 2) for b in range(blocks - 2) if not near[b + 1][b] and near[b + 1][b + 2]]
        back_one = [(b + 1, b) for b in range(blocks - 1) if (b + 1, b + 2) not in ahead]
        back_two = [(b + 2, b) for b in range(blocks - 2)]
        folded = terms[2] + moved(terms[1], "ctx", ahead)
        kv_sum = (
            kv_sum
            + moved(terms[1].astype(jnp.bfloat16), "ctx", back_one).astype(jnp.float32)
            + moved(folded.astype(jnp.bfloat16), "ctx", back_two).astype(jnp.float32)
        )
    query_grad = (
        (dq_acc * scale_factor)
        .astype(jnp.bfloat16)
        .reshape(1, tok_rows, kv_heads * group_size * HD)
    )
    kv_grad = kv_sum.astype(jnp.bfloat16)
    inner = lax.axis_size("sz")
    outer = lax.axis_size("sx")
    row_index = lax.axis_index("sx")
    col_index = lax.axis_index("sz")
    piece_count = tok_rows // PIECE
    route_table = route[0]
    seq_count = route_table.shape[0]
    piece_rows = kv_grad.reshape(piece_count, PIECE, kv_heads, 2 * HD)
    first_out = jnp.broadcast_to(piece_rows[None], (inner,) + piece_rows.shape)
    first_in = lax.all_to_all(first_out, "sz", split_axis=0, concat_axis=0, tiled=True)
    row_routes = lax.dynamic_slice_in_dim(route_table, row_index * inner, inner, 0)
    owners = jnp.arange(seq_count, dtype=jnp.int32)
    hits = (route_table[:, :, None] == owners[None, None, :]).astype(jnp.int32)
    sends = jnp.sum(hits, 1)
    ranks = jnp.cumsum(sends, 0) - sends
    row_ranks = lax.dynamic_slice_in_dim(ranks, row_index * inner, inner, 0)
    slot_ids = jnp.arange(2 * piece_count, dtype=jnp.int32)
    target_rows = jnp.arange(outer, dtype=jnp.int32)
    target_owner = target_rows * inner + col_index
    piece_owner = row_routes
    piece_rank = jnp.take_along_axis(row_ranks, piece_owner, axis=1)
    second_map = (
        (piece_owner[None, None, :, :] == target_owner[:, None, None, None])
        & (piece_rank[None, None, :, :] == slot_ids[None, :, None, None])
    ).astype(jnp.bfloat16)
    second_out = jnp.einsum(
        "tkzp,zpxhw->tkxhw", second_map, first_in, preferred_element_type=jnp.bfloat16
    )
    second_in = lax.all_to_all(second_out, "sx", split_axis=0, concat_axis=0, tiled=True)
    owned = second_in[0]
    for source in range(1, outer):
        owned = owned + second_in[source]
    return (query_grad, owned.reshape(1, 2 * piece_count * PIECE, kv_heads, 2 * HD))


def solution(mesh):
    seq_count = mesh.shape["seq"]
    inner = 8 if seq_count % 8 == 0 else 1
    split_mesh = Mesh(
        mesh.devices.reshape(mesh.shape["ctx"], seq_count // inner, inner, mesh.shape["head"]),
        ("ctx", "sx", "sz", "head"),
    )
    seq = ("sx", "sz")
    placed = (
        P(seq, "ctx", "head"),
        P(seq, "ctx", "head", None),
        P(seq, "ctx", "head"),
        P(seq, None),
        P("ctx", None, None),
    )
    ctx_count = mesh.shape["ctx"]
    heights = [mesh.devices[c, 0, 0].coords[2] for c in range(ctx_count)]
    near = [[heights[a] == heights[b] for b in range(ctx_count)] for a in range(ctx_count)]
    return jax.shard_map(
        functools.partial(shards, near),
        mesh=split_mesh,
        in_specs=placed,
        out_specs=(P(seq, "ctx", "head"), P(seq, "ctx", "head", None)),
        check_vma=False,
    )
```
